512 devices in a mesh: inp: 64 (over y_lo, z, x), tm: 8 (over y_hi, core).
Axes of the slice: x: 4, y: 8 (y_hi: 4, y_lo: 2; y = y_hi * 2 + y_lo), z: 8, core: 2. Of those that a mesh axis runs over, the one named last changes fastest.
Arguments:
- samples: bfloat16 [1024, 64, 1024], P('inp', 'tm'), may hold values from -8 to 8
- filter_taps: float32 [4, 1024], replicated, may hold values from -0.09375 to 0.09375
- partner_mask: int32 [2], replicated, may hold values from 1 to 63, as said below
Outputs:
- visibilities: float32 [1024, 3, 16, 1024], P('inp', None, None, 'tm')
The draws below stay inside these ranges and needn't reach their ends.
Inputs may be any that keep to these rules, and one draw needn't show every extreme that they name: `partner_mask`: the 2 masks are distinct and one of them is 63; in a round, input block p pairs with input block p XOR the mask.
All inputs are finite; a program needn't handle non-finite values.
Results may differ from the reference program's by a relative error of at most 0.0009.
Values may be sent and summed in bfloat16 or wider, within the bound.
No kernel may reach another device: no remote copies, remote signals or barrier semaphores. Data moves between devices by JAX's collectives and lax.ppermute only.
A program may use at most 64 MiB of HBM per device.

```python
import math
import jax
import jax.numpy as jnp
from jax import lax

NI = 1024
CH = 512
TAPS = 4
ROUNDS = 2
NFFT = 1024
IN_DEV = 16
NSPEC = 64
PAIRS = 3
N_INP = 64


def draw_samples(key, part):
    key_noise = jax.random.fold_in(key, 11)
    key_sky = jax.random.fold_in(key, 12)
    key_gain = jax.random.fold_in(key, 13)
    noise_part = jax.random.normal(key_noise, (NI, NSPEC, NFFT), jnp.float32)
    sky_signal = jax.random.normal(key_sky, (1, NSPEC, NFFT), jnp.float32)
    input_gain = jax.random.uniform(key_gain, (NI, 1, 1), jnp.float32, 0.5, 1.5)
    values = 0.6 * noise_part + 0.8 * input_gain * sky_signal
    return jnp.clip(values, -8.0, 8.0).astype(jnp.bfloat16)


def draw_partner_mask(key, part):
    others = jax.random.permutation(jax.random.fold_in(key, 5), N_INP - 2) + 1
    masks = jnp.concatenate([jnp.full((1,), N_INP - 1, jnp.int32), others[:ROUNDS - 1].astype(jnp.int32)])
    order = jax.random.permutation(jax.random.fold_in(key, 6), ROUNDS)
    return masks[order].astype(jnp.int32)


def noise(stream_key, extent, width, bound, held_as=jnp.bfloat16):
    return jnp.clip(width * jax.random.normal(stream_key, extent, jnp.float32), -bound, bound).astype(held_as)


def setup_inputs(seed: int = 0) -> dict:
    splits = jax.random.split(jax.random.key(seed), 4)
    return {
        "samples": draw_samples(jax.random.fold_in(splits[3], 71), 0),
        "filter_taps": noise(splits[1], (TAPS, NFFT), (TAPS * NFFT) ** -0.5, 0.09375, jnp.float32),
        "partner_mask": draw_partner_mask(jax.random.fold_in(splits[3], 71), 0),
    }


def dft_columns(n_fft):
    channels = n_fft // 2
    sample_ids = jnp.arange(n_fft, dtype=jnp.int32)[:, None]
    chan_ids = jnp.arange(channels, dtype=jnp.int32)[None, :]
    phase = ((sample_ids * chan_ids) % n_fft).astype(jnp.float32) * (2.0 * math.pi / n_fft)
    return jnp.concatenate([jnp.cos(phase), -jnp.sin(phase)], axis=1)


def cross_pairs(left, right, form):
    products = jnp.einsum(form, left.astype(jnp.float32), right.astype(jnp.float32), preferred_element_type=jnp.float32)
    real_part = products[..., 0, :, 0, :] + products[..., 1, :, 1, :]
    imag_part = products[..., 1, :, 0, :] - products[..., 0, :, 1, :]
    return jnp.stack([real_part, imag_part], axis=-2)


def reference(samples, filter_taps, partner_mask):
    dft_table = dft_columns(NFFT)
    grouped = samples.reshape(N_INP, IN_DEV, NSPEC, NFFT)

    def channelize(input_block):
        leading = jnp.zeros((IN_DEV, TAPS - 1, NFFT), input_block.dtype)
        frames = jnp.concatenate([leading, input_block], axis=1)
        filtered = jnp.zeros((IN_DEV, NSPEC, NFFT), jnp.float32)
        for tap_index in range(TAPS):
            filtered = filtered + filter_taps[tap_index][None, None, :].astype(jnp.float32) * frames[:, tap_index:tap_index + NSPEC, :].astype(jnp.float32)
        spectra = jnp.dot(filtered.reshape(IN_DEV * NSPEC, NFFT), dft_table, precision=lax.Precision.HIGHEST, preferred_element_type=jnp.float32)
        return spectra.astype(jnp.bfloat16).reshape(IN_DEV, NSPEC, 2, CH)

    spectra_all = lax.map(channelize, grouped)
    norm_scale = 1.0 / NSPEC

    def correlate(block_id):
        own_block = lax.dynamic_index_in_dim(spectra_all, block_id, 0, keepdims=False)
        pair_terms = [cross_pairs(own_block, own_block, "atic,btjc->aibjc")]
        for round_index in range(ROUNDS):
            partner_id = jnp.bitwise_xor(block_id, partner_mask[round_index]).astype(jnp.int32)
            partner = lax.dynamic_index_in_dim(spectra_all, partner_id, 0, keepdims=False)
            pair_terms.append(cross_pairs(own_block, partner, "atic,btjc->aibjc"))
        stacked = jnp.stack(pair_terms, axis=1) * norm_scale
        return stacked.reshape(IN_DEV, PAIRS, IN_DEV, 2 * CH)

    result = lax.map(correlate, jnp.arange(N_INP, dtype=jnp.int32))
    return result.reshape(NI, PAIRS, IN_DEV, 2 * CH)
```

```python
import math

import jax
import jax.numpy as jnp
from jax import lax
from jax.sharding import PartitionSpec as P

TAPS = 4
ROUNDS = 2


def shifted(block, axis, distance):
    devices = range(lax.axis_size(axis))
    route = [(i - distance, i) for i in devices if i - distance in devices]
    return lax.ppermute(block, axis, route)


def swapped_2(x, axis, bit):
    return lax.ppermute(x, axis, [(i, i ^ 1 << bit) for i in range(lax.axis_size(axis))])


def dft_columns(n_fft):
    channels = n_fft // 2
    sample_ids = jnp.arange(n_fft, dtype=jnp.int32)[:, None]
    chan_ids = jnp.arange(channels, dtype=jnp.int32)[None, :]
    phase = (sample_ids * chan_ids % n_fft).astype(jnp.float32) * (2.0 * math.pi / n_fft)
    return jnp.concatenate([jnp.cos(phase), -jnp.sin(phase)], axis=1)


def cross_batched(left, right):
    left_re = left[:, :, None, :, 0, :].astype(jnp.float32)
    left_im = left[:, :, None, :, 1, :].astype(jnp.float32)
    right_re = right[:, None, :, :, 0, :].astype(jnp.float32)
    right_im = right[:, None, :, :, 1, :].astype(jnp.float32)
    real_part = jnp.sum(left_re * right_re + left_im * right_im, axis=3)
    imag_part = jnp.sum(left_im * right_re - left_re * right_im, axis=3)
    return jnp.stack([real_part, imag_part], axis=-2)


def cross_single(left, right):
    return cross_batched(left[None], right[None])[0]


def channelize(samples, filter_taps):
    in_dev, spec_dev, n_fft = samples.shape
    history = shifted(samples[:, spec_dev - (TAPS - 1) :, :], "tm", 1)
    frames = jnp.concatenate([history, samples], axis=1)
    filtered = jnp.zeros((in_dev, spec_dev, n_fft), jnp.float32)
    for tap_index in range(TAPS):
        filtered = filtered + filter_taps[tap_index][None, None, :] * frames[
            :, tap_index : tap_index + spec_dev, :
        ].astype(jnp.float32)
    dft_table = dft_columns(n_fft)
    spectra = jnp.dot(
        filtered.reshape(in_dev * spec_dev, n_fft),
        dft_table,
        precision=lax.Precision.HIGHEST,
        preferred_element_type=jnp.float32,
    )
    return spectra.astype(jnp.bfloat16).reshape(in_dev, spec_dev, 2, n_fft // 2)


def on_device(samples, filter_taps, partner_mask):
    own_block = channelize(samples, filter_taps)
    in_dev, spec_dev, both_parts, channels = own_block.shape
    norm_scale = 1.0 / (spec_dev * lax.axis_size("tm"))
    bit_levels = lax.axis_size("inp").bit_length() - 1
    inp_size = lax.axis_size("inp")
    all_bits = inp_size - 1
    pair_terms = [cross_single(own_block, own_block)]
    full_partner = lax.ppermute(own_block, "inp", [(i, i ^ all_bits) for i in range(inp_size)])
    other_mask = jnp.where(partner_mask[0] == all_bits, partner_mask[1], partner_mask[0])
    branches = [
        (lambda m: lambda x: lax.ppermute(x, "inp", [(i, i ^ m) for i in range(inp_size)]))(m)
        for m in range(1, all_bits)
    ]
    other_partner = lax.switch(jnp.clip(other_mask - 1, 0, all_bits - 2), branches, own_block)
    for round_index in range(ROUNDS):
        is_full = partner_mask[round_index] == all_bits
        partner = jnp.where(is_full, full_partner, other_partner)
        pair_terms.append(cross_single(own_block, partner))
    partial_value = jnp.stack(pair_terms, axis=1) * norm_scale
    local_terms = partial_value.reshape(in_dev, ROUNDS + 1, in_dev, 2 * channels)
    return lax.psum_scatter(local_terms, "tm", scatter_dimension=3, tiled=True)


def solution(mesh):
    in_specs = (P("inp", "tm", None), P(), P())
    out_specs = P("inp", None, None, "tm")
    return jax.shard_map(
        on_device, mesh=mesh, in_specs=in_specs, out_specs=out_specs, check_vma=False
    )
```

```python
import math

import jax
import jax.numpy as jnp
from jax import lax
from jax.sharding import PartitionSpec as P

TAPS = 4
ROUNDS = 2


def shifted(block, axis, distance):
    devices = range(lax.axis_size(axis))
    route = [(i - distance, i) for i in devices if i - distance in devices]
    return lax.ppermute(block, axis, route)


def dft_columns(n_fft):
    channels = n_fft // 2
    sample_ids = jnp.arange(n_fft, dtype=jnp.int32)[:, None]
    chan_ids = jnp.arange(channels, dtype=jnp.int32)[None, :]
    phase = (sample_ids * chan_ids % n_fft).astype(jnp.float32) * (2.0 * math.pi / n_fft)
    return jnp.concatenate([jnp.cos(phase), -jnp.sin(phase)], axis=1)


def cross_batched(left, right):
    left_re = left[:, :, None, :, 0, :].astype(jnp.float32)
    left_im = left[:, :, None, :, 1, :].astype(jnp.float32)
    right_re = right[:, None, :, :, 0, :].astype(jnp.float32)
    right_im = right[:, None, :, :, 1, :].astype(jnp.float32)
    real_part = jnp.sum(left_re * right_re + left_im * right_im, axis=3)
    imag_part = jnp.sum(left_im * right_re - left_re * right_im, axis=3)
    return jnp.stack([real_part, imag_part], axis=-2)


def cross_single(left, right):
    return cross_batched(left[None], right[None])[0]


def channelize(samples, filter_taps):
    in_dev, spec_dev, n_fft = samples.shape
    history = shifted(samples[:, spec_dev - (TAPS - 1) :, :], "tm", 1)
    frames = jnp.concatenate([history, samples], axis=1)
    filtered = jnp.zeros((in_dev, spec_dev, n_fft), jnp.float32)
    for tap_index in range(TAPS):
        filtered = filtered + filter_taps[tap_index][None, None, :] * frames[
            :, tap_index : tap_index + spec_dev, :
        ].astype(jnp.float32)
    dft_table = dft_columns(n_fft)
    spectra = jnp.dot(
        filtered.reshape(in_dev * spec_dev, n_fft),
        dft_table,
        precision=lax.Precision.HIGHEST,
        preferred_element_type=jnp.float32,
    )
    return spectra.astype(jnp.bfloat16).reshape(in_dev, spec_dev, 2, n_fft // 2)


def on_device(samples, filter_taps, partner_mask):
    own_block = channelize(samples, filter_taps)
    in_dev, spec_dev, both_parts, channels = own_block.shape
    norm_scale = 1.0 / (spec_dev * lax.axis_size("tm"))
    inp_size = lax.axis_size("inp")
    all_bits = inp_size - 1

    def local_term(partner):
        term = cross_single(own_block, partner) * norm_scale
        return term.reshape(in_dev, in_dev, both_parts * channels)

    def reduced_term(term):
        return lax.psum_scatter(term, "tm", scatter_dimension=2, tiled=True)

    self_term = reduced_term(local_term(own_block))

    def exchange(m):
        def both(x):
            full = lax.ppermute(x, "inp", [(i, i ^ all_bits) for i in range(inp_size)])
            other = lax.ppermute(x, "inp", [(i, i ^ m) for i in range(inp_size)])
            return full, other
        return both

    other_mask = jnp.where(partner_mask[0] == all_bits, partner_mask[1], partner_mask[0])
    branches = [exchange(m) for m in range(1, all_bits)]
    full_partner, other_partner = lax.switch(
        jnp.clip(other_mask - 1, 0, all_bits - 2), branches, own_block
    )
    full_term = reduced_term(local_term(full_partner))
    other_term = reduced_term(local_term(other_partner))
    round_terms = []
    for round_index in range(ROUNDS):
        is_full = partner_mask[round_index] == all_bits
        round_terms.append(jnp.where(is_full, full_term, other_term))
    return jnp.stack([self_term] + round_terms, axis=1)


def solution(mesh):
    in_specs = (P("inp", "tm", None), P(), P())
    out_specs = P("inp", None, None, "tm")
    return jax.shard_map(
        on_device, mesh=mesh, in_specs=in_specs, out_specs=out_specs, check_vma=False
    )
```

```python
import math

import jax
import jax.numpy as jnp
from jax import lax
from jax.sharding import PartitionSpec as P

TAPS = 4
ROUNDS = 2


def shifted(block, axis, distance):
    devices = range(lax.axis_size(axis))
    route = [(i - distance, i) for i in devices if i - distance in devices]
    return lax.ppermute(block, axis, route)


def dft_columns(n_fft):
    channels = n_fft // 2
    sample_ids = jnp.arange(n_fft, dtype=jnp.int32)[:, None]
    chan_ids = jnp.arange(channels, dtype=jnp.int32)[None, :]
    phase = (sample_ids * chan_ids % n_fft).astype(jnp.float32) * (2.0 * math.pi / n_fft)
    return jnp.concatenate([jnp.cos(phase), -jnp.sin(phase)], axis=1)


def channelize(samples, filter_taps):
    in_dev, spec_dev, n_fft = samples.shape
    history = shifted(samples[:, spec_dev - (TAPS - 1) :, :], "tm", 1)
    frames = jnp.concatenate([history, samples], axis=1)
    filtered = jnp.zeros((in_dev, spec_dev, n_fft), jnp.float32)
    for tap_index in range(TAPS):
        filtered = filtered + filter_taps[tap_index][None, None, :] * frames[
            :, tap_index : tap_index + spec_dev, :
        ].astype(jnp.float32)
    dft_table = dft_columns(n_fft)
    spectra = jnp.dot(
        filtered.reshape(in_dev * spec_dev, n_fft),
        dft_table,
        precision=lax.Precision.HIGHEST,
        preferred_element_type=jnp.float32,
    )
    return spectra.astype(jnp.bfloat16).reshape(in_dev, spec_dev, 2, n_fft // 2)


def by_channel_chunk(block, tm_size):
    in_dev, spec_dev, both_parts, channels = block.shape
    chunks = tm_size // both_parts
    width = channels // chunks
    grouped = block.reshape(in_dev, spec_dev, both_parts, chunks, width)
    grouped = jnp.transpose(grouped, (3, 0, 1, 2, 4))
    send = jnp.concatenate([grouped] * (tm_size // chunks), axis=0)
    got = lax.all_to_all(send, "tm", 0, 0, tiled=True)
    got = jnp.transpose(got, (1, 0, 2, 3, 4))
    return got.reshape(in_dev, tm_size * spec_dev, both_parts, width)


def column_terms(left, right, imag_half):
    left_re = left[:, :, 0, :].astype(jnp.float32)
    left_im = left[:, :, 1, :].astype(jnp.float32)
    first = jnp.where(imag_half, left_im, left_re)
    second = jnp.where(imag_half, -left_re, left_im)
    right_re = right[None, :, :, 0, :].astype(jnp.float32)
    right_im = right[None, :, :, 1, :].astype(jnp.float32)
    return jnp.sum(first[:, None] * right_re + second[:, None] * right_im, axis=2)


def on_device(samples, filter_taps, partner_mask):
    spectra = channelize(samples, filter_taps)
    tm_size = lax.axis_size("tm")
    own_block = by_channel_chunk(spectra, tm_size)
    norm_scale = 1.0 / own_block.shape[1]
    inp_size = lax.axis_size("inp")
    all_bits = inp_size - 1
    imag_half = lax.axis_index("tm") >= tm_size // 2

    def exchange(m):
        def both(x):
            full = lax.ppermute(x, "inp", [(i, i ^ all_bits) for i in range(inp_size)])
            other = lax.ppermute(x, "inp", [(i, i ^ m) for i in range(inp_size)])
            return full, other
        return both

    other_mask = jnp.where(partner_mask[0] == all_bits, partner_mask[1], partner_mask[0])
    branches = [exchange(m) for m in range(1, all_bits)]
    full_partner, other_partner = lax.switch(
        jnp.clip(other_mask - 1, 0, all_bits - 2), branches, own_block
    )
    pair_terms = [column_terms(own_block, own_block, imag_half)]
    for round_index in range(ROUNDS):
        is_full = partner_mask[round_index] == all_bits
        partner = jnp.where(is_full, full_partner, other_partner)
        pair_terms.append(column_terms(own_block, partner, imag_half))
    return jnp.stack(pair_terms, axis=1) * norm_scale


def solution(mesh):
    in_specs = (P("inp", "tm", None), P(), P())
    out_specs = P("inp", None, None, "tm")
    return jax.shard_map(
        on_device, mesh=mesh, in_specs=in_specs, out_specs=out_specs, check_vma=False
    )
```

```python
import math

import jax
import jax.numpy as jnp
from jax import lax
from jax.sharding import PartitionSpec as P

TAPS = 4
ROUNDS = 2


def shifted(block, axis, distance):
    devices = range(lax.axis_size(axis))
    route = [(i - distance, i) for i in devices if i - distance in devices]
    return lax.ppermute(block, axis, route)


def dft_columns(n_fft):
    channels = n_fft // 2
    coarse = int(round(math.sqrt(n_fft)))
    fine = n_fft // coarse
    chan_ids = jnp.arange(channels, dtype=jnp.int32)[None, :]
    coarse_ids = jnp.arange(coarse, dtype=jnp.int32)[:, None]
    fine_ids = jnp.arange(fine, dtype=jnp.int32)[:, None]
    step = 2.0 * math.pi / n_fft
    coarse_phase = (fine * coarse_ids * chan_ids % n_fft).astype(jnp.float32) * step
    fine_phase = (fine_ids * chan_ids % n_fft).astype(jnp.float32) * step
    cos_a, sin_a = jnp.cos(coarse_phase)[:, None], jnp.sin(coarse_phase)[:, None]
    cos_b, sin_b = jnp.cos(fine_phase)[None], jnp.sin(fine_phase)[None]
    cos_ab = (cos_a * cos_b - sin_a * sin_b).reshape(n_fft, channels)
    sin_ab = (sin_a * cos_b + cos_a * sin_b).reshape(n_fft, channels)
    return jnp.concatenate([cos_ab, -sin_ab], axis=1)


def channelize(samples, filter_taps):
    in_dev, spec_dev, n_fft = samples.shape
    history = shifted(samples[:, spec_dev - (TAPS - 1) :, :], "tm", 1)
    frames = jnp.concatenate([history, samples], axis=1)
    filtered = jnp.zeros((in_dev, spec_dev, n_fft), jnp.float32)
    for tap_index in range(TAPS):
        filtered = filtered + filter_taps[tap_index][None, None, :] * frames[
            :, tap_index : tap_index + spec_dev, :
        ].astype(jnp.float32)
    dft_table = dft_columns(n_fft)
    spectra = jnp.dot(
        filtered.reshape(in_dev * spec_dev, n_fft),
        dft_table,
        precision=lax.Precision.HIGHEST,
        preferred_element_type=jnp.float32,
    )
    return spectra.astype(jnp.bfloat16).reshape(in_dev, spec_dev, 2, n_fft // 2)


def by_channel_chunk(block, tm_size):
    in_dev, spec_dev, both_parts, channels = block.shape
    chunks = tm_size // both_parts
    width = channels // chunks
    grouped = block.reshape(in_dev, spec_dev, both_parts, chunks, width)
    grouped = jnp.transpose(grouped, (3, 0, 1, 2, 4))
    send = jnp.concatenate([grouped] * (tm_size // chunks), axis=0)
    got = lax.all_to_all(send, "tm", 0, 0, tiled=True)
    got = jnp.transpose(got, (1, 0, 2, 3, 4))
    return got.reshape(in_dev, tm_size * spec_dev, both_parts, width)


def column_terms(left, right, imag_half):
    left_re = left[:, :, 0, :].astype(jnp.float32)
    left_im = left[:, :, 1, :].astype(jnp.float32)
    first = jnp.where(imag_half, left_im, left_re)
    second = jnp.where(imag_half, -left_re, left_im)
    right_re = right[None, :, :, 0, :].astype(jnp.float32)
    right_im = right[None, :, :, 1, :].astype(jnp.float32)
    return jnp.sum(first[:, None] * right_re + second[:, None] * right_im, axis=2)


def on_device(samples, filter_taps, partner_mask):
    spectra = channelize(samples, filter_taps)
    tm_size = lax.axis_size("tm")
    own_block = by_channel_chunk(spectra, tm_size)
    norm_scale = 1.0 / own_block.shape[1]
    inp_size = lax.axis_size("inp")
    all_bits = inp_size - 1
    imag_half = lax.axis_index("tm") >= tm_size // 2

    def exchange(m):
        def both(x):
            full = lax.ppermute(x, "inp", [(i, i ^ all_bits) for i in range(inp_size)])
            other = lax.ppermute(x, "inp", [(i, i ^ m) for i in range(inp_size)])
            return full, other
        return both

    other_mask = jnp.where(partner_mask[0] == all_bits, partner_mask[1], partner_mask[0])
    branches = [exchange(m) for m in range(1, all_bits)]
    full_partner, other_partner = lax.switch(
        jnp.clip(other_mask - 1, 0, all_bits - 2), branches, own_block
    )
    pair_terms = [column_terms(own_block, own_block, imag_half)]
    for round_index in range(ROUNDS):
        is_full = partner_mask[round_index] == all_bits
        partner = jnp.where(is_full, full_partner, other_partner)
        pair_terms.append(column_terms(own_block, partner, imag_half))
    return jnp.stack(pair_terms, axis=1) * norm_scale


def solution(mesh):
    in_specs = (P("inp", "tm", None), P(), P())
    out_specs = P("inp", None, None, "tm")
    return jax.shard_map(
        on_device, mesh=mesh, in_specs=in_specs, out_specs=out_specs, check_vma=False
    )
```

```python
import math

import jax
import jax.numpy as jnp
from jax import lax
from jax.sharding import PartitionSpec as P

TAPS = 4
ROUNDS = 2


def shifted(block, axis, distance):
    devices = range(lax.axis_size(axis))
    route = [(i - distance, i) for i in devices if i - distance in devices]
    return lax.ppermute(block, axis, route)


def dft_columns(n_fft):
    channels = n_fft // 2
    coarse = int(round(math.sqrt(n_fft)))
    fine = n_fft // coarse
    chan_ids = jnp.arange(channels, dtype=jnp.int32)[None, :]
    coarse_ids = jnp.arange(coarse, dtype=jnp.int32)[:, None]
    fine_ids = jnp.arange(fine, dtype=jnp.int32)[:, None]
    step = 2.0 * math.pi / n_fft
    coarse_phase = (fine * coarse_ids * chan_ids % n_fft).astype(jnp.float32) * step
    fine_phase = (fine_ids * chan_ids % n_fft).astype(jnp.float32) * step
    cos_a, sin_a = jnp.cos(coarse_phase)[:, None], jnp.sin(coarse_phase)[:, None]
    cos_b, sin_b = jnp.cos(fine_phase)[None], jnp.sin(fine_phase)[None]
    cos_ab = (cos_a * cos_b - sin_a * sin_b).reshape(n_fft, channels)
    sin_ab = (sin_a * cos_b + cos_a * sin_b).reshape(n_fft, channels)
    return jnp.concatenate([cos_ab, -sin_ab], axis=1)


def channelize(samples, filter_taps):
    in_dev, spec_dev, n_fft = samples.shape
    history = shifted(samples[:, spec_dev - (TAPS - 1) :, :], "tm", 1)
    frames = jnp.concatenate([history, samples], axis=1)
    filtered = jnp.zeros((in_dev, spec_dev, n_fft), jnp.float32)
    for tap_index in range(TAPS):
        filtered = filtered + filter_taps[tap_index][None, None, :] * frames[
            :, tap_index : tap_index + spec_dev, :
        ].astype(jnp.float32)
    dft_table = dft_columns(n_fft)
    spectra = jnp.dot(
        filtered.reshape(in_dev * spec_dev, n_fft),
        dft_table,
        precision=lax.Precision.HIGHEST,
        preferred_element_type=jnp.float32,
    )
    return spectra.astype(jnp.bfloat16).reshape(in_dev, spec_dev, 2, n_fft // 2)


def by_channel_chunk(block, tm_size):
    in_dev, spec_dev, both_parts, channels = block.shape
    chunks = tm_size // both_parts
    width = channels // chunks
    grouped = block.reshape(in_dev, spec_dev, both_parts, chunks, width)
    grouped = jnp.transpose(grouped, (3, 0, 1, 2, 4))
    send = jnp.concatenate([grouped] * (tm_size // chunks), axis=0)
    got = lax.all_to_all(send, "tm", 0, 0, tiled=True)
    got = jnp.transpose(got, (4, 1, 3, 0, 2))
    return got.reshape(width, in_dev, both_parts * tm_size * spec_dev)


def on_device(samples, filter_taps, partner_mask):
    spectra = channelize(samples, filter_taps)
    tm_size = lax.axis_size("tm")
    own_block = by_channel_chunk(spectra, tm_size)
    half = own_block.shape[2] // 2
    norm_scale = 1.0 / half
    inp_size = lax.axis_size("inp")
    all_bits = inp_size - 1
    imag_half = lax.axis_index("tm") >= tm_size // 2
    swapped = jnp.concatenate([own_block[..., half:], -own_block[..., :half]], axis=-1)
    left = jnp.where(imag_half, swapped, own_block)

    def column_terms(right):
        term = jnp.einsum("cix,cjx->ijc", left, right, preferred_element_type=jnp.float32)
        return term * norm_scale

    def exchange(m):
        def both(x):
            full = lax.ppermute(x, "inp", [(i, i ^ all_bits) for i in range(inp_size)])
            other = lax.ppermute(x, "inp", [(i, i ^ m) for i in range(inp_size)])
            return full, other
        return both

    other_mask = jnp.where(partner_mask[0] == all_bits, partner_mask[1], partner_mask[0])
    branches = [exchange(m) for m in range(1, all_bits)]
    full_partner, other_partner = lax.switch(
        jnp.clip(other_mask - 1, 0, all_bits - 2), branches, own_block
    )
    full_term = column_terms(full_partner)
    other_term = column_terms(other_partner)
    pair_terms = [column_terms(own_block)]
    for round_index in range(ROUNDS):
        is_full = partner_mask[round_index] == all_bits
        pair_terms.append(jnp.where(is_full, full_term, other_term))
    return jnp.stack(pair_terms, axis=1)


def solution(mesh):
    in_specs = (P("inp", "tm", None), P(), P())
    out_specs = P("inp", None, None, "tm")
    return jax.shard_map(
        on_device, mesh=mesh, in_specs=in_specs, out_specs=out_specs, check_vma=False
    )
```

```python
import math

import jax
import jax.numpy as jnp
from jax import lax
from jax.sharding import PartitionSpec as P

TAPS = 4
ROUNDS = 2


def shifted(block, axis, distance):
    devices = range(lax.axis_size(axis))
    route = [(i - distance, i) for i in devices if i - distance in devices]
    return lax.ppermute(block, axis, route)


def dft_columns(n_fft):
    channels = n_fft // 2
    coarse = int(round(math.sqrt(n_fft)))
    fine = n_fft // coarse
    chan_ids = jnp.arange(channels, dtype=jnp.int32)[None, :]
    coarse_ids = jnp.arange(coarse, dtype=jnp.int32)[:, None]
    fine_ids = jnp.arange(fine, dtype=jnp.int32)[:, None]
    step = 2.0 * math.pi / n_fft
    coarse_phase = (fine * coarse_ids * chan_ids % n_fft).astype(jnp.float32) * step
    fine_phase = (fine_ids * chan_ids % n_fft).astype(jnp.float32) * step
    cos_a, sin_a = jnp.cos(coarse_phase)[:, None], jnp.sin(coarse_phase)[:, None]
    cos_b, sin_b = jnp.cos(fine_phase)[None], jnp.sin(fine_phase)[None]
    cos_ab = (cos_a * cos_b - sin_a * sin_b).reshape(n_fft, channels)
    sin_ab = (sin_a * cos_b + cos_a * sin_b).reshape(n_fft, channels)
    return jnp.concatenate([cos_ab, -sin_ab], axis=1)


def channelize(samples, filter_taps):
    in_dev, spec_dev, n_fft = samples.shape
    history = shifted(samples[:, spec_dev - (TAPS - 1) :, :], "tm", 1)
    frames = jnp.concatenate([history, samples], axis=1)
    filtered = jnp.zeros((in_dev, spec_dev, n_fft), jnp.float32)
    for tap_index in range(TAPS):
        filtered = filtered + filter_taps[tap_index][None, None, :] * frames[
            :, tap_index : tap_index + spec_dev, :
        ].astype(jnp.float32)
    dft_table = dft_columns(n_fft)
    spectra = jnp.dot(
        filtered.reshape(in_dev * spec_dev, n_fft),
        dft_table,
        precision=lax.Precision.HIGHEST,
        preferred_element_type=jnp.float32,
    )
    return spectra.astype(jnp.bfloat16).reshape(in_dev, spec_dev, 2, n_fft // 2)


def by_channel_chunk(block, tm_size):
    in_dev, spec_dev, both_parts, channels = block.shape
    chunks = tm_size // both_parts
    width = channels // chunks
    grouped = block.reshape(in_dev, spec_dev, both_parts, chunks, width)
    grouped = jnp.transpose(grouped, (3, 0, 1, 2, 4))
    send = jnp.concatenate([grouped] * (tm_size // chunks), axis=0)
    got = lax.all_to_all(send, "tm", 0, 0, tiled=True)
    got = jnp.transpose(got, (1, 0, 2, 3, 4))
    return got.reshape(in_dev, tm_size * spec_dev, both_parts, width)


def on_device(samples, filter_taps, partner_mask):
    spectra = channelize(samples, filter_taps)
    tm_size = lax.axis_size("tm")
    own_block = by_channel_chunk(spectra, tm_size)
    norm_scale = 1.0 / own_block.shape[1]
    inp_size = lax.axis_size("inp")
    all_bits = inp_size - 1
    imag_half = lax.axis_index("tm") >= tm_size // 2
    swapped = jnp.concatenate([own_block[:, :, 1:], -own_block[:, :, :1]], axis=2)
    left = jnp.where(imag_half, swapped, own_block)
    in_dev, frames, both_parts, width = own_block.shape
    left = left.reshape(in_dev, frames * both_parts, width)

    def column_terms(right):
        right = right.reshape(in_dev, frames * both_parts, width)
        term = jnp.einsum("ixc,jxc->ijc", left, right, preferred_element_type=jnp.float32)
        return term * norm_scale

    def exchange(m):
        def both(x):
            full = lax.ppermute(x, "inp", [(i, i ^ all_bits) for i in range(inp_size)])
            other = lax.ppermute(x, "inp", [(i, i ^ m) for i in range(inp_size)])
            return full, other
        return both

    other_mask = jnp.where(partner_mask[0] == all_bits, partner_mask[1], partner_mask[0])
    branches = [exchange(m) for m in range(1, all_bits)]
    full_partner, other_partner = lax.switch(
        jnp.clip(other_mask - 1, 0, all_bits - 2), branches, own_block
    )
    full_term = column_terms(full_partner)
    other_term = column_terms(other_partner)
    pair_terms = [column_terms(own_block)]
    for round_index in range(ROUNDS):
        is_full = partner_mask[round_index] == all_bits
        pair_terms.append(jnp.where(is_full, full_term, other_term))
    return jnp.stack(pair_terms, axis=1)


def solution(mesh):
    in_specs = (P("inp", "tm", None), P(), P())
    out_specs = P("inp", None, None, "tm")
    return jax.shard_map(
        on_device, mesh=mesh, in_specs=in_specs, out_specs=out_specs, check_vma=False
    )
```

```python
import math

import jax
import jax.numpy as jnp
from jax import lax
from jax.sharding import PartitionSpec as P

TAPS = 4
ROUNDS = 2


def shifted(block, axis, distance):
    devices = range(lax.axis_size(axis))
    route = [(i - distance, i) for i in devices if i - distance in devices]
    return lax.ppermute(block, axis, route)


def dft_columns(n_fft):
    channels = n_fft // 2
    coarse = int(round(math.sqrt(n_fft)))
    fine = n_fft // coarse
    chan_ids = jnp.arange(channels, dtype=jnp.int32)[None, :]
    coarse_ids = jnp.arange(coarse, dtype=jnp.int32)[:, None]
    fine_ids = jnp.arange(fine, dtype=jnp.int32)[:, None]
    step = 2.0 * math.pi / n_fft
    coarse_phase = (fine * coarse_ids * chan_ids % n_fft).astype(jnp.float32) * step
    fine_phase = (fine_ids * chan_ids % n_fft).astype(jnp.float32) * step
    cos_a, sin_a = jnp.cos(coarse_phase)[:, None], jnp.sin(coarse_phase)[:, None]
    cos_b, sin_b = jnp.cos(fine_phase)[None], jnp.sin(fine_phase)[None]
    cos_ab = (cos_a * cos_b - sin_a * sin_b).reshape(n_fft, channels)
    sin_ab = (sin_a * cos_b + cos_a * sin_b).reshape(n_fft, channels)
    return jnp.concatenate([cos_ab, -sin_ab], axis=1)


def filter_frames(frames, filter_taps, count):
    filtered = jnp.zeros((frames.shape[0], count, frames.shape[2]), jnp.float32)
    for tap_index in range(TAPS):
        filtered = filtered + filter_taps[tap_index][None, None, :] * frames[
            :, tap_index : tap_index + count, :
        ].astype(jnp.float32)
    return filtered


def spectra_of(filtered, dft_table):
    in_dev, count, n_fft = filtered.shape
    spectra = jnp.dot(
        filtered.reshape(in_dev * count, n_fft),
        dft_table,
        precision=lax.Precision.HIGHEST,
        preferred_element_type=jnp.float32,
    )
    return spectra.reshape(in_dev, count, n_fft)


def channelize(samples, filter_taps):
    in_dev, spec_dev, n_fft = samples.shape
    lead = TAPS - 1
    history = shifted(samples[:, spec_dev - lead :, :], "tm", 1)
    blank = jnp.zeros((in_dev, lead, n_fft), samples.dtype)
    dft_table = dft_columns(n_fft)
    local_part = spectra_of(
        filter_frames(jnp.concatenate([blank, samples], axis=1), filter_taps, spec_dev), dft_table
    )
    history_part = spectra_of(
        filter_frames(jnp.concatenate([history, blank], axis=1), filter_taps, lead), dft_table
    )
    spectra = jnp.concatenate([local_part[:, :lead] + history_part, local_part[:, lead:]], axis=1)
    return spectra.astype(jnp.bfloat16).reshape(in_dev, spec_dev, 2, n_fft // 2)


def by_channel_chunk(block, tm_size):
    in_dev, spec_dev, both_parts, channels = block.shape
    chunks = tm_size // both_parts
    width = channels // chunks
    grouped = block.reshape(in_dev, spec_dev, both_parts, chunks, width)
    grouped = jnp.transpose(grouped, (3, 0, 1, 2, 4))
    send = jnp.concatenate([grouped] * (tm_size // chunks), axis=0)
    got = lax.all_to_all(send, "tm", 0, 0, tiled=True)
    got = jnp.transpose(got, (1, 0, 2, 3, 4))
    return got.reshape(in_dev, tm_size * spec_dev, both_parts, width)


def column_terms(left, right, imag_half):
    left_re = left[:, :, 0, :].astype(jnp.float32)
    left_im = left[:, :, 1, :].astype(jnp.float32)
    first = jnp.where(imag_half, left_im, left_re)
    second = jnp.where(imag_half, -left_re, left_im)
    right_re = right[None, :, :, 0, :].astype(jnp.float32)
    right_im = right[None, :, :, 1, :].astype(jnp.float32)
    return jnp.sum(first[:, None] * right_re + second[:, None] * right_im, axis=2)


def on_device(samples, filter_taps, partner_mask):
    spectra = channelize(samples, filter_taps)
    tm_size = lax.axis_size("tm")
    own_block = by_channel_chunk(spectra, tm_size)
    norm_scale = 1.0 / own_block.shape[1]
    inp_size = lax.axis_size("inp")
    all_bits = inp_size - 1
    imag_half = lax.axis_index("tm") >= tm_size // 2

    def exchange(m):
        def both(x):
            full = lax.ppermute(x, "inp", [(i, i ^ all_bits) for i in range(inp_size)])
            other = lax.ppermute(x, "inp", [(i, i ^ m) for i in range(inp_size)])
            return full, other
        return both

    other_mask = jnp.where(partner_mask[0] == all_bits, partner_mask[1], partner_mask[0])
    branches = [exchange(m) for m in range(1, all_bits)]
    full_partner, other_partner = lax.switch(
        jnp.clip(other_mask - 1, 0, all_bits - 2), branches, own_block
    )
    full_term = column_terms(own_block, full_partner, imag_half)
    other_term = column_terms(own_block, other_partner, imag_half)
    pair_terms = [column_terms(own_block, own_block, imag_half)]
    for round_index in range(ROUNDS):
        is_full = partner_mask[round_index] == all_bits
        pair_terms.append(jnp.where(is_full, full_term, other_term))
    return jnp.stack(pair_terms, axis=1) * norm_scale


def solution(mesh):
    in_specs = (P("inp", "tm", None), P(), P())
    out_specs = P("inp", None, None, "tm")
    return jax.shard_map(
        on_device, mesh=mesh, in_specs=in_specs, out_specs=out_specs, check_vma=False
    )
```

```python
import math

import jax
import jax.numpy as jnp
from jax import lax
from jax.sharding import PartitionSpec as P

TAPS = 4
ROUNDS = 2


def shifted(block, axis, distance):
    devices = range(lax.axis_size(axis))
    route = [(i - distance, i) for i in devices if i - distance in devices]
    return lax.ppermute(block, axis, route)


def dft_columns(n_fft):
    channels = n_fft // 2
    coarse = int(round(math.sqrt(n_fft)))
    fine = n_fft // coarse
    chan_ids = jnp.arange(channels, dtype=jnp.int32)[None, :]
    coarse_ids = jnp.arange(coarse, dtype=jnp.int32)[:, None]
    fine_ids = jnp.arange(fine, dtype=jnp.int32)[:, None]
    step = 2.0 * math.pi / n_fft
    coarse_phase = (fine * coarse_ids * chan_ids % n_fft).astype(jnp.float32) * step
    fine_phase = (fine_ids * chan_ids % n_fft).astype(jnp.float32) * step
    cos_a, sin_a = jnp.cos(coarse_phase)[:, None], jnp.sin(coarse_phase)[:, None]
    cos_b, sin_b = jnp.cos(fine_phase)[None], jnp.sin(fine_phase)[None]
    cos_ab = (cos_a * cos_b - sin_a * sin_b).reshape(n_fft, channels)
    sin_ab = (sin_a * cos_b + cos_a * sin_b).reshape(n_fft, channels)
    return jnp.concatenate([cos_ab, -sin_ab], axis=1)


def channelize(samples, filter_taps):
    in_dev, spec_dev, n_fft = samples.shape
    history = shifted(samples[:, spec_dev - (TAPS - 1) :, :], "tm", 1)
    frames = jnp.concatenate([history, samples], axis=1)
    filtered = jnp.zeros((in_dev, spec_dev, n_fft), jnp.float32)
    for tap_index in range(TAPS):
        filtered = filtered + filter_taps[tap_index][None, None, :] * frames[
            :, tap_index : tap_index + spec_dev, :
        ].astype(jnp.float32)
    dft_table = dft_columns(n_fft)
    spectra = jnp.dot(
        filtered.reshape(in_dev * spec_dev, n_fft),
        dft_table,
        precision=lax.Precision.HIGHEST,
        preferred_element_type=jnp.float32,
    )
    return spectra.astype(jnp.bfloat16).reshape(in_dev, spec_dev, 2, n_fft // 2)


def by_channel_chunk(block, tm_size):
    in_dev, spec_dev, both_parts, channels = block.shape
    chunks = tm_size // both_parts
    width = channels // chunks
    grouped = block.reshape(in_dev, spec_dev, both_parts, chunks, width)
    grouped = jnp.transpose(grouped, (3, 0, 1, 2, 4))
    send = jnp.concatenate([grouped] * (tm_size // chunks), axis=0)
    got = lax.all_to_all(send, "tm", 0, 0, tiled=True)
    got = jnp.transpose(got, (1, 0, 2, 3, 4))
    return got.reshape(in_dev, tm_size * spec_dev, both_parts, width)


def on_device(samples, filter_taps, partner_mask):
    spectra = channelize(samples, filter_taps)
    tm_size = lax.axis_size("tm")
    own_block = by_channel_chunk(spectra, tm_size)
    norm_scale = 1.0 / own_block.shape[1]
    inp_size = lax.axis_size("inp")
    all_bits = inp_size - 1
    imag_half = lax.axis_index("tm") >= tm_size // 2
    in_dev, frames, both_parts, width = own_block.shape

    def channel_major(block):
        return jnp.transpose(block, (3, 0, 2, 1)).reshape(width, in_dev, both_parts * frames)

    own_major = channel_major(own_block)
    half = own_major.shape[2] // 2
    swapped = jnp.concatenate([own_major[..., half:], -own_major[..., :half]], axis=-1)
    left = jnp.where(imag_half, swapped, own_major)

    def column_terms(right):
        term = jnp.einsum("cix,cjx->ijc", left, channel_major(right), preferred_element_type=jnp.float32)
        return term * norm_scale

    def exchange(m):
        def both(x):
            full = lax.ppermute(x, "inp", [(i, i ^ all_bits) for i in range(inp_size)])
            other = lax.ppermute(x, "inp", [(i, i ^ m) for i in range(inp_size)])
            return full, other
        return both

    other_mask = jnp.where(partner_mask[0] == all_bits, partner_mask[1], partner_mask[0])
    branches = [exchange(m) for m in range(1, all_bits)]
    full_partner, other_partner = lax.switch(
        jnp.clip(other_mask - 1, 0, all_bits - 2), branches, own_block
    )
    full_term = column_terms(full_partner)
    other_term = column_terms(other_partner)
    pair_terms = [column_terms(own_block)]
    for round_index in range(ROUNDS):
        is_full = partner_mask[round_index] == all_bits
        pair_terms.append(jnp.where(is_full, full_term, other_term))
    return jnp.stack(pair_terms, axis=1)


def solution(mesh):
    in_specs = (P("inp", "tm", None), P(), P())
    out_specs = P("inp", None, None, "tm")
    return jax.shard_map(
        on_device, mesh=mesh, in_specs=in_specs, out_specs=out_specs, check_vma=False
    )
```

```python
import math

import jax
import jax.numpy as jnp
from jax import lax
from jax.sharding import PartitionSpec as P

TAPS = 4
ROUNDS = 2


def shifted(block, axis, distance):
    devices = range(lax.axis_size(axis))
    route = [(i - distance, i) for i in devices if i - distance in devices]
    return lax.ppermute(block, axis, route)


def dft_columns(n_fft):
    channels = n_fft // 2
    coarse = int(round(math.sqrt(n_fft)))
    fine = n_fft // coarse
    chan_ids = jnp.arange(channels, dtype=jnp.int32)[None, :]
    coarse_ids = jnp.arange(coarse, dtype=jnp.int32)[:, None]
    fine_ids = jnp.arange(fine, dtype=jnp.int32)[:, None]
    step = 2.0 * math.pi / n_fft
    coarse_phase = (fine * coarse_ids * chan_ids % n_fft).astype(jnp.float32) * step
    fine_phase = (fine_ids * chan_ids % n_fft).astype(jnp.float32) * step
    cos_a, sin_a = jnp.cos(coarse_phase)[:, None], jnp.sin(coarse_phase)[:, None]
    cos_b, sin_b = jnp.cos(fine_phase)[None], jnp.sin(fine_phase)[None]
    cos_ab = (cos_a * cos_b - sin_a * sin_b).reshape(n_fft, channels)
    sin_ab = (sin_a * cos_b + cos_a * sin_b).reshape(n_fft, channels)
    return jnp.concatenate([cos_ab, -sin_ab], axis=1)


def channelize(samples, filter_taps):
    in_dev, spec_dev, n_fft = samples.shape
    history = shifted(samples[:, spec_dev - (TAPS - 1) :, :], "tm", 1)
    frames = jnp.concatenate([history, samples], axis=1)
    filtered = jnp.zeros((in_dev, spec_dev, n_fft), jnp.float32)
    for tap_index in range(TAPS):
        filtered = filtered + filter_taps[tap_index][None, None, :] * frames[
            :, tap_index : tap_index + spec_dev, :
        ].astype(jnp.float32)
    dft_table = dft_columns(n_fft)
    spectra = jnp.dot(
        filtered.reshape(in_dev * spec_dev, n_fft),
        dft_table,
        precision=lax.Precision.HIGHEST,
        preferred_element_type=jnp.float32,
    )
    return spectra.astype(jnp.bfloat16).reshape(in_dev, spec_dev, 2, n_fft // 2)


def by_channel_chunk(block, tm_size):
    in_dev, spec_dev, both_parts, channels = block.shape
    chunks = tm_size // both_parts
    width = channels // chunks
    grouped = block.reshape(in_dev, spec_dev, both_parts, chunks, width)
    grouped = jnp.transpose(grouped, (3, 0, 1, 2, 4))
    send = jnp.concatenate([grouped] * (tm_size // chunks), axis=0)
    got = lax.all_to_all(send, "tm", 0, 0, tiled=True)
    got = jnp.transpose(got, (4, 1, 3, 0, 2))
    return got.reshape(width, in_dev, both_parts * tm_size * spec_dev)


def on_device(samples, filter_taps, partner_mask):
    spectra = channelize(samples, filter_taps)
    tm_size = lax.axis_size("tm")
    in_dev = spectra.shape[0]
    own_block = by_channel_chunk(spectra, tm_size)
    half = own_block.shape[2] // 2
    norm_scale = 1.0 / half
    inp_size = lax.axis_size("inp")
    all_bits = inp_size - 1
    imag_half = lax.axis_index("tm") >= tm_size // 2
    swapped = jnp.concatenate([own_block[..., half:], -own_block[..., :half]], axis=-1)
    left = jnp.where(imag_half, swapped, own_block)

    def column_terms(right):
        term = jnp.einsum("cix,cjx->ijc", left, right, preferred_element_type=jnp.float32)
        return term * norm_scale

    def exchange(m):
        def both(x):
            full = lax.ppermute(x, "inp", [(i, i ^ all_bits) for i in range(inp_size)])
            other = lax.ppermute(x, "inp", [(i, i ^ m) for i in range(inp_size)])
            return full, other
        return both

    other_mask = jnp.where(partner_mask[0] == all_bits, partner_mask[1], partner_mask[0])
    branches = [exchange(m) for m in range(1, all_bits)]
    full_spectra, other_spectra = lax.switch(
        jnp.clip(other_mask - 1, 0, all_bits - 2), branches, spectra
    )
    partners = by_channel_chunk(jnp.concatenate([full_spectra, other_spectra], axis=0), tm_size)
    full_term = column_terms(partners[:, :in_dev])
    other_term = column_terms(partners[:, in_dev:])
    pair_terms = [column_terms(own_block)]
    for round_index in range(ROUNDS):
        is_full = partner_mask[round_index] == all_bits
        pair_terms.append(jnp.where(is_full, full_term, other_term))
    return jnp.stack(pair_terms, axis=1)


def solution(mesh):
    in_specs = (P("inp", "tm", None), P(), P())
    out_specs = P("inp", None, None, "tm")
    return jax.shard_map(
        on_device, mesh=mesh, in_specs=in_specs, out_specs=out_specs, check_vma=False
    )
```

```python
import math

import jax
import jax.numpy as jnp
from jax import lax
from jax.sharding import PartitionSpec as P

TAPS = 4
ROUNDS = 2


def shifted(block, axis, distance):
    devices = range(lax.axis_size(axis))
    route = [(i - distance, i) for i in devices if i - distance in devices]
    return lax.ppermute(block, axis, route)


def dft_columns(n_fft):
    channels = n_fft // 2
    coarse = int(round(math.sqrt(n_fft)))
    fine = n_fft // coarse
    chan_ids = jnp.arange(channels, dtype=jnp.int32)[None, :]
    coarse_ids = jnp.arange(coarse, dtype=jnp.int32)[:, None]
    fine_ids = jnp.arange(fine, dtype=jnp.int32)[:, None]
    step = 2.0 * math.pi / n_fft
    coarse_phase = (fine * coarse_ids * chan_ids % n_fft).astype(jnp.float32) * step
    fine_phase = (fine_ids * chan_ids % n_fft).astype(jnp.float32) * step
    cos_a, sin_a = jnp.cos(coarse_phase)[:, None], jnp.sin(coarse_phase)[:, None]
    cos_b, sin_b = jnp.cos(fine_phase)[None], jnp.sin(fine_phase)[None]
    cos_ab = (cos_a * cos_b - sin_a * sin_b).reshape(n_fft, channels)
    sin_ab = (sin_a * cos_b + cos_a * sin_b).reshape(n_fft, channels)
    return jnp.concatenate([cos_ab, -sin_ab], axis=1)


def channelize(samples, filter_taps):
    in_dev, spec_dev, n_fft = samples.shape
    history = shifted(samples[:, spec_dev - (TAPS - 1) :, :], "tm", 1)
    frames = jnp.concatenate([history, samples], axis=1)
    filtered = jnp.zeros((in_dev, spec_dev, n_fft), jnp.float32)
    for tap_index in range(TAPS):
        filtered = filtered + filter_taps[tap_index][None, None, :] * frames[
            :, tap_index : tap_index + spec_dev, :
        ].astype(jnp.float32)
    dft_table = dft_columns(n_fft)
    spectra = jnp.dot(
        filtered.reshape(in_dev * spec_dev, n_fft),
        dft_table,
        precision=lax.Precision.HIGHEST,
        preferred_element_type=jnp.float32,
    )
    return spectra.astype(jnp.bfloat16).reshape(in_dev, spec_dev, 2, n_fft // 2)


def by_channel_chunk(block, tm_size):
    in_dev, spec_dev, both_parts, channels = block.shape
    chunks = tm_size // both_parts
    width = channels // chunks
    grouped = block.reshape(in_dev, spec_dev, both_parts, chunks, width)
    grouped = jnp.transpose(grouped, (3, 0, 1, 2, 4))
    send = jnp.concatenate([grouped] * (tm_size // chunks), axis=0)
    got = lax.all_to_all(send, "tm", 0, 0, tiled=True)
    got = jnp.transpose(got, (4, 1, 3, 0, 2))
    return got.reshape(width, in_dev, both_parts * tm_size * spec_dev)


def on_device(samples, filter_taps, partner_mask):
    spectra = channelize(samples, filter_taps)
    tm_size = lax.axis_size("tm")
    own_block = by_channel_chunk(spectra, tm_size)
    half = own_block.shape[2] // 2
    norm_scale = 1.0 / half
    inp_size = lax.axis_size("inp")
    all_bits = inp_size - 1
    imag_half = lax.axis_index("tm") >= tm_size // 2
    swapped = jnp.concatenate([own_block[..., half:], -own_block[..., :half]], axis=-1)
    left = jnp.where(imag_half, swapped, own_block)

    def column_terms(right):
        term = jnp.einsum("cix,cjx->ijc", left, right, preferred_element_type=jnp.float32)
        return term * norm_scale

    def exchange(m):
        def both(x):
            full = lax.ppermute(x, "inp", [(i, i ^ all_bits) for i in range(inp_size)])
            other = lax.ppermute(x, "inp", [(i, i ^ m) for i in range(inp_size)])
            return full, other
        return both

    other_mask = jnp.where(partner_mask[0] == all_bits, partner_mask[1], partner_mask[0])
    branches = [exchange(m) for m in range(1, all_bits)]
    full_partner, other_partner = lax.switch(
        jnp.clip(other_mask - 1, 0, all_bits - 2), branches, own_block
    )
    blocks = [own_block]
    for round_index in range(ROUNDS):
        is_full = partner_mask[round_index] == all_bits
        blocks.append(jnp.where(is_full, full_partner, other_partner))
    terms = column_terms(jnp.concatenate(blocks, axis=1))
    return terms.reshape(terms.shape[0], ROUNDS + 1, -1, terms.shape[2])


def solution(mesh):
    in_specs = (P("inp", "tm", None), P(), P())
    out_specs = P("inp", None, None, "tm")
    return jax.shard_map(
        on_device, mesh=mesh, in_specs=in_specs, out_specs=out_specs, check_vma=False
    )
```

```python
import math

import jax
import jax.numpy as jnp
from jax import lax
from jax.sharding import PartitionSpec as P

TAPS = 4
ROUNDS = 2


def shifted(block, axis, distance):
    devices = range(lax.axis_size(axis))
    route = [(i - distance, i) for i in devices if i - distance in devices]
    return lax.ppermute(block, axis, route)


def dft_columns(n_fft):
    channels = n_fft // 2
    coarse = int(round(math.sqrt(n_fft)))
    fine = n_fft // coarse
    chan_ids = jnp.arange(channels, dtype=jnp.int32)[None, :]
    coarse_ids = jnp.arange(coarse, dtype=jnp.int32)[:, None]
    fine_ids = jnp.arange(fine, dtype=jnp.int32)[:, None]
    step = 2.0 * math.pi / n_fft
    coarse_phase = (fine * coarse_ids * chan_ids % n_fft).astype(jnp.float32) * step
    fine_phase = (fine_ids * chan_ids % n_fft).astype(jnp.float32) * step
    cos_a, sin_a = jnp.cos(coarse_phase)[:, None], jnp.sin(coarse_phase)[:, None]
    cos_b, sin_b = jnp.cos(fine_phase)[None], jnp.sin(fine_phase)[None]
    cos_ab = (cos_a * cos_b - sin_a * sin_b).reshape(n_fft, channels)
    sin_ab = (sin_a * cos_b + cos_a * sin_b).reshape(n_fft, channels)
    return jnp.concatenate([cos_ab, -sin_ab], axis=1)


def channelize(samples, filter_taps):
    in_dev, spec_dev, n_fft = samples.shape
    history = shifted(samples[:, spec_dev - (TAPS - 1) :, :], "tm", 1)
    frames = jnp.concatenate([history, samples], axis=1)
    filtered = jnp.zeros((in_dev, spec_dev, n_fft), jnp.float32)
    for tap_index in range(TAPS):
        filtered = filtered + filter_taps[tap_index][None, None, :] * frames[
            :, tap_index : tap_index + spec_dev, :
        ].astype(jnp.float32)
    dft_table = dft_columns(n_fft)
    spectra = jnp.dot(
        filtered.reshape(in_dev * spec_dev, n_fft),
        dft_table,
        precision=lax.Precision.HIGH,
        preferred_element_type=jnp.float32,
    )
    return spectra.astype(jnp.bfloat16).reshape(in_dev, spec_dev, 2, n_fft // 2)


def by_channel_chunk(block, tm_size):
    in_dev, spec_dev, both_parts, channels = block.shape
    chunks = tm_size // both_parts
    width = channels // chunks
    grouped = block.reshape(in_dev, spec_dev, both_parts, chunks, width)
    grouped = jnp.transpose(grouped, (3, 0, 1, 2, 4))
    send = jnp.concatenate([grouped] * (tm_size // chunks), axis=0)
    got = lax.all_to_all(send, "tm", 0, 0, tiled=True)
    got = jnp.transpose(got, (4, 1, 3, 0, 2))
    return got.reshape(width, in_dev, both_parts * tm_size * spec_dev)


def on_device(samples, filter_taps, partner_mask):
    spectra = channelize(samples, filter_taps)
    tm_size = lax.axis_size("tm")
    own_block = by_channel_chunk(spectra, tm_size)
    half = own_block.shape[2] // 2
    norm_scale = 1.0 / half
    inp_size = lax.axis_size("inp")
    all_bits = inp_size - 1
    imag_half = lax.axis_index("tm") >= tm_size // 2
    swapped = jnp.concatenate([own_block[..., half:], -own_block[..., :half]], axis=-1)
    left = jnp.where(imag_half, swapped, own_block)

    def column_terms(right):
        term = jnp.einsum("cix,cjx->ijc", left, right, preferred_element_type=jnp.float32)
        return term * norm_scale

    def exchange(m):
        def both(x):
            full = lax.ppermute(x, "inp", [(i, i ^ all_bits) for i in range(inp_size)])
            other = lax.ppermute(x, "inp", [(i, i ^ m) for i in range(inp_size)])
            return full, other
        return both

    other_mask = jnp.where(partner_mask[0] == all_bits, partner_mask[1], partner_mask[0])
    branches = [exchange(m) for m in range(1, all_bits)]
    full_partner, other_partner = lax.switch(
        jnp.clip(other_mask - 1, 0, all_bits - 2), branches, own_block
    )
    blocks = [own_block]
    for round_index in range(ROUNDS):
        is_full = partner_mask[round_index] == all_bits
        blocks.append(jnp.where(is_full, full_partner, other_partner))
    terms = column_terms(jnp.concatenate(blocks, axis=1))
    return terms.reshape(terms.shape[0], ROUNDS + 1, -1, terms.shape[2])


def solution(mesh):
    in_specs = (P("inp", "tm", None), P(), P())
    out_specs = P("inp", None, None, "tm")
    return jax.shard_map(
        on_device, mesh=mesh, in_specs=in_specs, out_specs=out_specs, check_vma=False
    )
```
